256 devices in a mesh: doc: 16 (over z_hi, x, core), word: 16 (over y, z_lo).
Axes of the slice: x: 4, y: 4, z: 8 (z_hi: 2, z_lo: 4; z = z_hi * 4 + z_lo), core: 2. Of those that a mesh axis runs over, the one named last changes fastest.
Arguments:
- counts: int32 [8192, 8192], P('doc', 'word'), may hold values from 0 to 29
- topics: float32 [8192, 256], P(('word', 'doc')), may hold values from 0.05 to 0.5
- latent: float32 [8192, 8192], P('doc', 'word'), may hold values from 0.5 to 30
- dual_latent: float32 [8192, 8192], P('doc', 'word'), may hold values from -3 to 3
- doc_plus: float32 [8192, 256], P(('doc', 'word')), may hold values from 0 to 0.5
- topic_plus: float32 [8192, 256], P(('word', 'doc')), may hold values from 0 to 3
- dual_doc: float32 [8192, 256], P(('doc', 'word')), may hold values from -2 to 2
- dual_topic: float32 [8192, 256], P(('word', 'doc')), may hold values from -2 to 2
Outputs:
- doc_factor_out: float32 [8192, 256], P(('doc', 'word'))
- topics_out: float32 [8192, 256], P(('word', 'doc'))
- latent_out: float32 [8192, 8192], P('doc', 'word')
- dual_latent_out: float32 [8192, 8192], P('doc', 'word')
- doc_plus_out: float32 [8192, 256], P(('doc', 'word'))
- topic_plus_out: float32 [8192, 256], P(('word', 'doc'))
- dual_doc_out: float32 [8192, 256], P(('doc', 'word'))
- dual_topic_out: float32 [8192, 256], P(('word', 'doc'))
The draws below stay inside these ranges and needn't reach their ends.
All inputs are finite; a program needn't handle non-finite values. Where the reference program divides by a largest or mean magnitude, that divisor is 1e-20 or more.
Results may differ from the reference program's by a relative error of at most 0.00075.
Values sent between devices are 32-bit elements; how exact they have to be, the bound alone decides.
No kernel may reach another device: no remote copies, remote signals or barrier semaphores. Data moves between devices by JAX's collectives and lax.ppermute only.
A program may use at most 64 MiB of HBM per device.

```python
import math
import jax
import jax.numpy as jnp
from jax import lax

K = 256
ITERS = 2
NEWTON = 18
DOCS = 8192
WORDS = 8192


def place_ends(result, own_key, least, largest):
    shape = result.shape
    place = [jax.random.randint(jax.random.fold_in(own_key, axis), (), 0, shape[axis]) for axis in range(len(shape))]
    result = result.at[tuple(place)].set(least)
    longest = shape.index(max(shape))
    place[longest] = (place[longest] + 1) % shape[longest]
    return result.at[tuple(place)].set(largest)


def block_levels(own_key, shape, pieces, least, high):
    gain = 1.0
    for position, blocks in pieces:
        heights = jax.random.uniform(jax.random.fold_in(jax.random.fold_in(own_key, 6), position), (blocks,), jnp.float32, least / len(pieces), high / len(pieces))
        gain = gain * jnp.repeat(jnp.exp(heights), shape[position] // blocks).reshape((-1,) + (1,) * (len(shape) - 1 - position))
    return gain


def bell_draw(stream_key, shape, scale, most, pieces=(), kind=jnp.bfloat16):
    factor_of = block_levels(stream_key, shape, pieces, -0.22, 0.18) if pieces else 1.0
    array = jax.random.normal(stream_key, shape, jnp.float32) * scale * factor_of
    return jnp.minimum(jnp.maximum(array, -most), most).astype(kind)


def setup_inputs(seed: int = 0) -> dict:
    key_list = jax.random.split(jax.random.key(seed), 9)
    return {
        "counts": place_ends(jax.random.randint(key_list[0], (DOCS, WORDS), 0, 30), jax.random.fold_in(key_list[0], 1), 0, 29).astype(jnp.int32),
        "topics": jnp.clip(jnp.exp(math.log(0.5) - 2.3025851 * jax.random.uniform(key_list[1], (WORDS, K), jnp.float32) ** block_levels(key_list[1], (WORDS, K), ((0, 256),), -0.2, 0.2)), 0.05, 0.5),
        "latent": jnp.clip(jnp.exp(math.log(30.0) - 4.0943446 * jax.random.uniform(key_list[2], (DOCS, WORDS), jnp.float32) ** block_levels(key_list[2], (DOCS, WORDS), ((0, 16), (1, 16)), -0.2, 0.2)), 0.5, 30.0),
        "dual_latent": bell_draw(key_list[3], (DOCS, WORDS), 0.5, 3.0, ((0, 16), (1, 16)), jnp.float32),
        "doc_plus": jnp.clip(0.5 * jax.random.uniform(key_list[4], (DOCS, K), jnp.float32) ** block_levels(key_list[4], (DOCS, K), ((0, 256),), -0.2, 0.2), 0.0, 0.5),
        "topic_plus": jnp.clip(3.0 * jax.random.uniform(key_list[5], (WORDS, K), jnp.float32) ** block_levels(key_list[5], (WORDS, K), ((0, 256),), -0.2, 0.2), 0.0, 3.0),
        "dual_doc": bell_draw(key_list[6], (DOCS, K), 0.3, 2.0, ((0, 256),), jnp.float32),
        "dual_topic": bell_draw(key_list[7], (WORDS, K), 0.3, 2.0, ((0, 256),), jnp.float32),
    }


def product(left, right):
    return jnp.dot(left, right, precision=lax.Precision.HIGHEST, preferred_element_type=jnp.float32)

def product_left(left, right):
    return lax.dot_general(left, right, (((0,), (0,)), ((), ())), precision=lax.Precision.HIGHEST, preferred_element_type=jnp.float32)

def product_right(left, right):
    return lax.dot_general(left, right, (((1,), (1,)), ((), ())), precision=lax.Precision.HIGHEST, preferred_element_type=jnp.float32)

def invert(gram):
    identity_mat = jnp.eye(gram.shape[0], dtype=jnp.float32)
    matrix = gram + identity_mat
    row_bound = jnp.max(lax.optimization_barrier(jnp.sum(jnp.abs(matrix), axis=1)))
    approx = identity_mat / row_bound
    for newton_step in range(NEWTON):
        approx = product(approx, 2.0 * identity_mat - product(matrix, approx))
    return approx

def reference(counts, topics, latent, dual_latent, doc_plus, topic_plus, dual_doc, dual_topic):
    counts_float = counts.astype(jnp.float32)
    doc_factor = doc_plus
    for iteration in range(ITERS):
        merged = latent + dual_latent
        doc_factor = product(product(merged, topics) + doc_plus - dual_doc, invert(product_left(topics, topics)))
        topics = product(product_left(merged, doc_factor) + topic_plus - dual_topic, invert(product_left(doc_factor, doc_factor)))
        rebuilt = product_right(doc_factor, topics)
        shifted = rebuilt - dual_latent - 1.0
        latent = 0.5 * (shifted + jnp.sqrt(shifted * shifted + 4.0 * counts_float))
        doc_plus = jnp.maximum(doc_factor + dual_doc, 0.0)
        topic_plus = jnp.maximum(topics + dual_topic, 0.0)
        dual_latent = dual_latent + latent - rebuilt
        dual_doc = dual_doc + doc_factor - doc_plus
        dual_topic = dual_topic + topics - topic_plus
    return (doc_factor, topics, latent, dual_latent, doc_plus, topic_plus, dual_doc, dual_topic)
```

```python
import jax
import jax.numpy as jnp
from jax import lax
from jax.sharding import PartitionSpec as P

ITERS = 2
NEWTON = 18
ALL = ("doc", "word")


def partners(axis, bit):
    return [(i, i ^ bit) for i in range(lax.axis_size(axis))]


def exchanged_sum(x, axis):
    bit = 1
    while bit < lax.axis_size(axis):
        x = x + lax.ppermute(x, axis, partners(axis, bit))
        bit *= 2
    return x


def exchanged_gather(x, axis):
    me = lax.axis_index(axis)
    bit = 1
    while bit < lax.axis_size(axis):
        other = lax.ppermute(x, axis, partners(axis, bit))
        x = jnp.where((me & bit) == 0, jnp.concatenate([x, other]), jnp.concatenate([other, x]))
        bit *= 2
    return x


def own_rows(tile, axis, rows):
    return lax.dynamic_slice_in_dim(tile, lax.axis_index(axis) * rows, rows, 0)


def product(left, right):
    return jnp.dot(left, right, precision=lax.Precision.HIGHEST, preferred_element_type=jnp.float32)


def product_left(left, right):
    return lax.dot_general(
        left,
        right,
        (((0,), (0,)), ((), ())),
        precision=lax.Precision.HIGHEST,
        preferred_element_type=jnp.float32,
    )


def product_right(left, right):
    return lax.dot_general(
        left,
        right,
        (((1,), (1,)), ((), ())),
        precision=lax.Precision.HIGHEST,
        preferred_element_type=jnp.float32,
    )


def invert(gram):
    identity_mat = jnp.eye(gram.shape[0], dtype=jnp.float32)
    matrix = gram + identity_mat
    row_bound = jnp.max(jnp.sum(jnp.abs(matrix), axis=1))
    approx = identity_mat / row_bound
    for newton_step in range(NEWTON):
        approx = product(approx, 2.0 * identity_mat - product(matrix, approx))
    return approx


def per_device(counts, topics, latent, dual_latent, doc_plus, topic_plus, dual_doc, dual_topic):
    counts_float = counts.astype(jnp.float32)
    rows, k = topics.shape
    topic_side = exchanged_gather(jnp.concatenate([topics, topic_plus, dual_topic], axis=1), "doc")
    topic_tile, topic_plus_tile, dual_topic_tile = (topic_side[:, i * k : (i + 1) * k] for i in range(3))
    doc_side = exchanged_gather(jnp.concatenate([doc_plus, dual_doc], axis=1), "word")
    doc_plus_tile, dual_doc_tile = doc_side[:, :k], doc_side[:, k:]
    gram_topic = exchanged_sum(product_left(topic_tile, topic_tile), "word")
    for iteration in range(ITERS):
        merged = latent + dual_latent
        inverse_topic = invert(gram_topic)
        doc_rhs_tile = exchanged_sum(product(merged, topic_tile), "word") + doc_plus_tile - dual_doc_tile
        doc_tile = product(doc_rhs_tile, inverse_topic)
        gram_doc = exchanged_sum(product_left(doc_tile, doc_tile), "doc")
        inverse_doc = invert(gram_doc)
        topic_rhs_tile = exchanged_sum(product_left(merged, doc_tile), "doc") + topic_plus_tile - dual_topic_tile
        topic_tile = product(topic_rhs_tile, inverse_doc)
        if iteration + 1 < ITERS:
            gram_topic = exchanged_sum(product_left(topic_tile, topic_tile), "word")
        rebuilt = product_right(doc_tile, topic_tile)
        shifted = rebuilt - dual_latent - 1.0
        latent = 0.5 * (shifted + jnp.sqrt(shifted * shifted + 4.0 * counts_float))
        doc_plus_tile = jnp.maximum(doc_tile + dual_doc_tile, 0.0)
        topic_plus_tile = jnp.maximum(topic_tile + dual_topic_tile, 0.0)
        dual_latent = dual_latent + latent - rebuilt
        dual_doc_tile = dual_doc_tile + doc_tile - doc_plus_tile
        dual_topic_tile = dual_topic_tile + topic_tile - topic_plus_tile
    doc_rows = [own_rows(t, "word", rows) for t in (doc_tile, doc_plus_tile, dual_doc_tile)]
    topic_rows = [own_rows(t, "doc", rows) for t in (topic_tile, topic_plus_tile, dual_topic_tile)]
    return (doc_rows[0], topic_rows[0], latent, dual_latent, doc_rows[1], topic_rows[1], doc_rows[2], topic_rows[2])


def solution(mesh):
    in_specs = (
        P("doc", "word"),
        P(("word", "doc"), None),
        P("doc", "word"),
        P("doc", "word"),
        P(("doc", "word"), None),
        P(("word", "doc"), None),
        P(("doc", "word"), None),
        P(("word", "doc"), None),
    )
    out_specs = (
        P(("doc", "word"), None),
        P(("word", "doc"), None),
        P("doc", "word"),
        P("doc", "word"),
        P(("doc", "word"), None),
        P(("word", "doc"), None),
        P(("doc", "word"), None),
        P(("word", "doc"), None),
    )
    return jax.shard_map(
        per_device, mesh=mesh, in_specs=in_specs, out_specs=out_specs, check_vma=False
    )
```

```python
import jax
import jax.numpy as jnp
from jax import lax
from jax.sharding import PartitionSpec as P

ITERS = 2
NEWTON = 18
ALL = ("doc", "word")


def joined_along(pieces, dim):
    pieces = jnp.moveaxis(pieces, 0, dim)
    dims = pieces.shape
    return pieces.reshape(*dims[:dim], dims[dim] * dims[dim + 1], *dims[dim + 2 :])


def gathered_copies(x, axis):
    count = lax.axis_size(axis)
    pieces = lax.all_to_all(jnp.broadcast_to(x[None], (count, *x.shape)), axis, 0, 0, tiled=True)
    return joined_along(pieces, 0)


def summed_on_arrival(x, axis):
    count = lax.axis_size(axis)
    pieces = lax.all_to_all(x.reshape(count, x.shape[0] // count, *x.shape[1:]), axis, 0, 0, tiled=True)
    return jnp.sum(pieces, axis=0)


def summed_everywhere(x, axis):
    return gathered_copies(summed_on_arrival(x, axis), axis)


def own_rows(tile, axis, rows):
    return lax.dynamic_slice_in_dim(tile, lax.axis_index(axis) * rows, rows, 0)


def product(left, right):
    return jnp.dot(left, right, precision=lax.Precision.HIGHEST, preferred_element_type=jnp.float32)


def product_left(left, right):
    return lax.dot_general(
        left,
        right,
        (((0,), (0,)), ((), ())),
        precision=lax.Precision.HIGHEST,
        preferred_element_type=jnp.float32,
    )


def product_right(left, right):
    return lax.dot_general(
        left,
        right,
        (((1,), (1,)), ((), ())),
        precision=lax.Precision.HIGHEST,
        preferred_element_type=jnp.float32,
    )


def invert(gram):
    identity_mat = jnp.eye(gram.shape[0], dtype=jnp.float32)
    matrix = gram + identity_mat
    row_bound = jnp.max(jnp.sum(jnp.abs(matrix), axis=1))
    approx = identity_mat / row_bound
    for newton_step in range(NEWTON):
        approx = product(approx, 2.0 * identity_mat - product(matrix, approx))
    return approx


def per_device(counts, topics, latent, dual_latent, doc_plus, topic_plus, dual_doc, dual_topic):
    counts_float = counts.astype(jnp.float32)
    rows, k = topics.shape
    topic_side = gathered_copies(jnp.concatenate([topics, topic_plus, dual_topic], axis=1), "doc")
    topic_tile, topic_plus_tile, dual_topic_tile = (topic_side[:, i * k : (i + 1) * k] for i in range(3))
    doc_side = gathered_copies(jnp.concatenate([doc_plus, dual_doc], axis=1), "word")
    doc_plus_tile, dual_doc_tile = doc_side[:, :k], doc_side[:, k:]
    for iteration in range(ITERS):
        merged = latent + dual_latent
        word_summed = summed_everywhere(
            jnp.concatenate([product(merged, topic_tile), product_left(topic_tile, topic_tile)]), "word"
        )
        doc_rhs_tile = word_summed[: merged.shape[0]] + doc_plus_tile - dual_doc_tile
        inverse_topic = invert(word_summed[merged.shape[0] :])
        doc_tile = product(doc_rhs_tile, inverse_topic)
        doc_summed = summed_everywhere(
            jnp.concatenate([product_left(merged, doc_tile), product_left(doc_tile, doc_tile)]), "doc"
        )
        topic_rhs_tile = doc_summed[: merged.shape[1]] + topic_plus_tile - dual_topic_tile
        inverse_doc = invert(doc_summed[merged.shape[1] :])
        topic_tile = product(topic_rhs_tile, inverse_doc)
        rebuilt = product_right(doc_tile, topic_tile)
        shifted = rebuilt - dual_latent - 1.0
        latent = 0.5 * (shifted + jnp.sqrt(shifted * shifted + 4.0 * counts_float))
        doc_plus_tile = jnp.maximum(doc_tile + dual_doc_tile, 0.0)
        topic_plus_tile = jnp.maximum(topic_tile + dual_topic_tile, 0.0)
        dual_latent = dual_latent + latent - rebuilt
        dual_doc_tile = dual_doc_tile + doc_tile - doc_plus_tile
        dual_topic_tile = dual_topic_tile + topic_tile - topic_plus_tile
    doc_rows = [own_rows(t, "word", rows) for t in (doc_tile, doc_plus_tile, dual_doc_tile)]
    topic_rows = [own_rows(t, "doc", rows) for t in (topic_tile, topic_plus_tile, dual_topic_tile)]
    return (doc_rows[0], topic_rows[0], latent, dual_latent, doc_rows[1], topic_rows[1], doc_rows[2], topic_rows[2])


def solution(mesh):
    in_specs = (
        P("doc", "word"),
        P(("word", "doc"), None),
        P("doc", "word"),
        P("doc", "word"),
        P(("doc", "word"), None),
        P(("word", "doc"), None),
        P(("doc", "word"), None),
        P(("word", "doc"), None),
    )
    out_specs = (
        P(("doc", "word"), None),
        P(("word", "doc"), None),
        P("doc", "word"),
        P("doc", "word"),
        P(("doc", "word"), None),
        P(("word", "doc"), None),
        P(("doc", "word"), None),
        P(("word", "doc"), None),
    )
    return jax.shard_map(
        per_device, mesh=mesh, in_specs=in_specs, out_specs=out_specs, check_vma=False
    )
```

```python
import jax
import jax.numpy as jnp
from jax import lax
from jax.sharding import PartitionSpec as P

ITERS = 2
NEWTON = 18


def joined_along(pieces, dim):
    pieces = jnp.moveaxis(pieces, 0, dim)
    dims = pieces.shape
    return pieces.reshape(*dims[:dim], dims[dim] * dims[dim + 1], *dims[dim + 2 :])


def copy_for_each(x, axis):
    count = lax.axis_size(axis)
    return lax.all_to_all(jnp.broadcast_to(x[None], (count, *x.shape)), axis, 0, 0, tiled=True)


def gathered_copies(x, axis, dim):
    return joined_along(copy_for_each(x, axis), dim)


def split_up(x, dim, count):
    dims = x.shape
    pieces = x.reshape(*dims[:dim], count, dims[dim] // count, *dims[dim + 1 :])
    return jnp.moveaxis(pieces, dim, 0)


def summed_on_arrival(x, axis, dim):
    count = lax.axis_size(axis)
    pieces = lax.all_to_all(split_up(x, dim, count), axis, 0, 0, tiled=True)
    return jnp.sum(pieces, axis=0)


def rows_for(lines, count):
    spare = -len(lines) % count
    return jnp.pad(lines, [(0, spare)] + [(0, 0)] * (lines.ndim - 1))


def nested_sum(x, axes):
    lines = x.reshape(-1, x.shape[-1])
    own = summed_on_arrival(rows_for(lines, lax.axis_size(axes)), axes, 0)
    whole = gathered_copies(own, axes, 0)
    return whole[: len(lines)].reshape(x.shape)


def product(left, right):
    return jnp.dot(left, right, precision=lax.Precision.HIGHEST, preferred_element_type=jnp.float32)


def product_left(left, right):
    return lax.dot_general(
        left,
        right,
        (((0,), (0,)), ((), ())),
        precision=lax.Precision.HIGHEST,
        preferred_element_type=jnp.float32,
    )


def product_right(left, right):
    return lax.dot_general(
        left,
        right,
        (((1,), (1,)), ((), ())),
        precision=lax.Precision.HIGHEST,
        preferred_element_type=jnp.float32,
    )


def invert(gram):
    identity_mat = jnp.eye(gram.shape[0], dtype=jnp.float32)
    matrix = gram + identity_mat
    row_bound = jnp.max(jnp.sum(jnp.abs(matrix), axis=1))
    approx = identity_mat / row_bound
    def newton_step(step, approx):
        return product(approx, 2.0 * identity_mat - product(matrix, approx))

    return lax.fori_loop(0, NEWTON, newton_step, approx)


def gather_topics(topics):
    return gathered_copies(topics, "doc", 0)


def per_device(counts, topics, latent, dual_latent, doc_plus, topic_plus, dual_doc, dual_topic):
    counts_float = counts.astype(jnp.float32)
    doc_factor = doc_plus
    topic_tile = gather_topics(topics)
    for iteration in range(ITERS):
        merged = latent + dual_latent
        gram_topic = nested_sum(product_left(topic_tile, topic_tile), "word")

        def doc_term(first_row, row_count, merged=merged, topic_tile=topic_tile):
            return product(merged, topic_tile)

        doc_sums = summed_on_arrival(
            doc_term(jnp.int32(0), doc_plus.shape[0] * lax.axis_size("word")), "word", 0
        )
        doc_factor = product(doc_sums + doc_plus - dual_doc, invert(gram_topic))
        doc_tile = gathered_copies(doc_factor, "word", 0)
        gram_doc = nested_sum(product_left(doc_tile, doc_tile), "doc")
        inverse_doc = invert(gram_doc)

        def word_term(first_row, row_count, merged=merged, doc_tile=doc_tile):
            return product_left(merged, doc_tile)

        word_sums = summed_on_arrival(
            word_term(jnp.int32(0), topics.shape[0] * lax.axis_size("doc")), "doc", 0
        )
        topics = product(word_sums + topic_plus - dual_topic, inverse_doc)
        topic_tile = gather_topics(topics)
        rebuilt = product_right(doc_tile, topic_tile)
        shifted = rebuilt - dual_latent - 1.0
        latent = 0.5 * (shifted + jnp.sqrt(shifted * shifted + 4.0 * counts_float))
        doc_plus = jnp.maximum(doc_factor + dual_doc, 0.0)
        topic_plus = jnp.maximum(topics + dual_topic, 0.0)
        dual_latent = dual_latent + latent - rebuilt
        dual_doc = dual_doc + doc_factor - doc_plus
        dual_topic = dual_topic + topics - topic_plus
    return (doc_factor, topics, latent, dual_latent, doc_plus, topic_plus, dual_doc, dual_topic)


def solution(mesh):
    in_specs = (
        P("doc", "word"),
        P(("word", "doc"), None),
        P("doc", "word"),
        P("doc", "word"),
        P(("doc", "word"), None),
        P(("word", "doc"), None),
        P(("doc", "word"), None),
        P(("word", "doc"), None),
    )
    out_specs = (
        P(("doc", "word"), None),
        P(("word", "doc"), None),
        P("doc", "word"),
        P("doc", "word"),
        P(("doc", "word"), None),
        P(("word", "doc"), None),
        P(("doc", "word"), None),
        P(("word", "doc"), None),
    )
    return jax.shard_map(
        per_device, mesh=mesh, in_specs=in_specs, out_specs=out_specs, check_vma=False
    )
```

```python
import jax
import jax.numpy as jnp
from jax import lax
from jax.sharding import PartitionSpec as P

ITERS = 2
NEWTON = 18


def joined_along(pieces, dim):
    pieces = jnp.moveaxis(pieces, 0, dim)
    dims = pieces.shape
    return pieces.reshape(*dims[:dim], dims[dim] * dims[dim + 1], *dims[dim + 2 :])


def copy_for_each(x, axis):
    count = lax.axis_size(axis)
    return lax.all_to_all(jnp.broadcast_to(x[None], (count, *x.shape)), axis, 0, 0, tiled=True)


def gathered_copies(x, axis, dim):
    return joined_along(copy_for_each(x, axis), dim)


def split_up(x, dim, count):
    dims = x.shape
    pieces = x.reshape(*dims[:dim], count, dims[dim] // count, *dims[dim + 1 :])
    return jnp.moveaxis(pieces, dim, 0)


def summed_on_arrival(x, axis, dim):
    count = lax.axis_size(axis)
    pieces = lax.all_to_all(split_up(x, dim, count), axis, 0, 0, tiled=True)
    return jnp.sum(pieces, axis=0)


def rows_for(lines, count):
    spare = -len(lines) % count
    return jnp.pad(lines, [(0, spare)] + [(0, 0)] * (lines.ndim - 1))


def nested_sum(x, axes):
    lines = x.reshape(-1, x.shape[-1])
    own = summed_on_arrival(rows_for(lines, lax.axis_size(axes)), axes, 0)
    whole = gathered_copies(own, axes, 0)
    return whole[: len(lines)].reshape(x.shape)


def product(left, right):
    return jnp.dot(left, right, precision=lax.Precision.HIGHEST, preferred_element_type=jnp.float32)


def product_left(left, right):
    return lax.dot_general(
        left,
        right,
        (((0,), (0,)), ((), ())),
        precision=lax.Precision.HIGHEST,
        preferred_element_type=jnp.float32,
    )


def product_right(left, right):
    return lax.dot_general(
        left,
        right,
        (((1,), (1,)), ((), ())),
        precision=lax.Precision.HIGHEST,
        preferred_element_type=jnp.float32,
    )


def invert(gram):
    identity_mat = jnp.eye(gram.shape[0], dtype=jnp.float32)
    matrix = gram + identity_mat
    row_bound = jnp.max(jnp.sum(jnp.abs(matrix), axis=1))
    approx = identity_mat / row_bound
    for newton_step in range(NEWTON):
        approx = product(approx, 2.0 * identity_mat - product(matrix, approx))
    return approx


def gather_topics(topics):
    return gathered_copies(topics, "doc", 0)


def per_device(counts, topics, latent, dual_latent, doc_plus, topic_plus, dual_doc, dual_topic):
    counts_float = counts.astype(jnp.float32)
    doc_factor = doc_plus
    topic_tile = gather_topics(topics)
    for iteration in range(ITERS):
        merged = latent + dual_latent
        gram_topic = nested_sum(product_left(topic_tile, topic_tile), "word")

        def doc_term(first_row, row_count, merged=merged, topic_tile=topic_tile):
            return product(merged, topic_tile)

        doc_sums = summed_on_arrival(
            doc_term(jnp.int32(0), doc_plus.shape[0] * lax.axis_size("word")), "word", 0
        )
        doc_rhs = doc_sums + doc_plus - dual_doc
        doc_rhs_tile = gathered_copies(doc_rhs, "word", 0)
        inverse_topic = invert(gram_topic)
        doc_factor = product(doc_rhs, inverse_topic)
        doc_tile = product(doc_rhs_tile, inverse_topic)
        gram_doc = nested_sum(product_left(doc_tile, doc_tile), "doc")
        inverse_doc = invert(gram_doc)

        def word_term(first_row, row_count, merged=merged, doc_tile=doc_tile):
            return product_left(merged, doc_tile)

        word_sums = summed_on_arrival(
            word_term(jnp.int32(0), topics.shape[0] * lax.axis_size("doc")), "doc", 0
        )
        topic_rhs = word_sums + topic_plus - dual_topic
        topic_rhs_tile = gathered_copies(topic_rhs, "doc", 0)
        topics = product(topic_rhs, inverse_doc)
        topic_tile = product(topic_rhs_tile, inverse_doc)
        rebuilt = product_right(doc_tile, topic_tile)
        shifted = rebuilt - dual_latent - 1.0
        latent = 0.5 * (shifted + jnp.sqrt(shifted * shifted + 4.0 * counts_float))
        doc_plus = jnp.maximum(doc_factor + dual_doc, 0.0)
        topic_plus = jnp.maximum(topics + dual_topic, 0.0)
        dual_latent = dual_latent + latent - rebuilt
        dual_doc = dual_doc + doc_factor - doc_plus
        dual_topic = dual_topic + topics - topic_plus
    return (doc_factor, topics, latent, dual_latent, doc_plus, topic_plus, dual_doc, dual_topic)


def solution(mesh):
    in_specs = (
        P("doc", "word"),
        P(("word", "doc"), None),
        P("doc", "word"),
        P("doc", "word"),
        P(("doc", "word"), None),
        P(("word", "doc"), None),
        P(("doc", "word"), None),
        P(("word", "doc"), None),
    )
    out_specs = (
        P(("doc", "word"), None),
        P(("word", "doc"), None),
        P("doc", "word"),
        P("doc", "word"),
        P(("doc", "word"), None),
        P(("word", "doc"), None),
        P(("doc", "word"), None),
        P(("word", "doc"), None),
    )
    return jax.shard_map(
        per_device, mesh=mesh, in_specs=in_specs, out_specs=out_specs, check_vma=False
    )
```

```python
import jax
import jax.numpy as jnp
from jax import lax
from jax.sharding import PartitionSpec as P

ITERS = 2
NEWTON = 18


def joined_along(pieces, dim):
    pieces = jnp.moveaxis(pieces, 0, dim)
    dims = pieces.shape
    return pieces.reshape(*dims[:dim], dims[dim] * dims[dim + 1], *dims[dim + 2 :])


def copy_for_each(x, axis):
    count = lax.axis_size(axis)
    return lax.all_to_all(jnp.broadcast_to(x[None], (count, *x.shape)), axis, 0, 0, tiled=True)


def gathered_copies(x, axis, dim):
    return joined_along(copy_for_each(x, axis), dim)


def split_up(x, dim, count):
    dims = x.shape
    pieces = x.reshape(*dims[:dim], count, dims[dim] // count, *dims[dim + 1 :])
    return jnp.moveaxis(pieces, dim, 0)


def summed_on_arrival(x, axis, dim):
    count = lax.axis_size(axis)
    pieces = lax.all_to_all(split_up(x, dim, count), axis, 0, 0, tiled=True)
    return jnp.sum(pieces, axis=0)


def rows_for(lines, count):
    spare = -len(lines) % count
    return jnp.pad(lines, [(0, spare)] + [(0, 0)] * (lines.ndim - 1))


def nested_sum(x, axes):
    lines = x.reshape(-1, x.shape[-1])
    own = summed_on_arrival(rows_for(lines, lax.axis_size(axes)), axes, 0)
    whole = gathered_copies(own, axes, 0)
    return whole[: len(lines)].reshape(x.shape)


def exchanged_sum(x, axis):
    count = lax.axis_size(axis)
    bit = 1
    while bit < count:
        x = x + lax.ppermute(x, axis, [(i, i ^ bit) for i in range(count)])
        bit *= 2
    return x


def product(left, right):
    return jnp.dot(left, right, precision=lax.Precision.HIGHEST, preferred_element_type=jnp.float32)


def product_left(left, right):
    return lax.dot_general(
        left,
        right,
        (((0,), (0,)), ((), ())),
        precision=lax.Precision.HIGHEST,
        preferred_element_type=jnp.float32,
    )


def product_right(left, right):
    return lax.dot_general(
        left,
        right,
        (((1,), (1,)), ((), ())),
        precision=lax.Precision.HIGHEST,
        preferred_element_type=jnp.float32,
    )


def invert(gram):
    identity_mat = jnp.eye(gram.shape[0], dtype=jnp.float32)
    matrix = gram + identity_mat
    row_bound = jnp.max(jnp.sum(jnp.abs(matrix), axis=1))
    approx = identity_mat / row_bound
    for newton_step in range(NEWTON):
        approx = product(approx, 2.0 * identity_mat - product(matrix, approx))
    return approx


def gather_topics(topics):
    return gathered_copies(topics, "doc", 0)


def per_device(counts, topics, latent, dual_latent, doc_plus, topic_plus, dual_doc, dual_topic):
    counts_float = counts.astype(jnp.float32)
    doc_factor = doc_plus
    topic_tile = gather_topics(topics)
    for iteration in range(ITERS):
        merged = latent + dual_latent
        gram_topic = exchanged_sum(product_left(topic_tile, topic_tile), "word")

        def doc_term(first_row, row_count, merged=merged, topic_tile=topic_tile):
            return product(merged, topic_tile)

        doc_sums = summed_on_arrival(
            doc_term(jnp.int32(0), doc_plus.shape[0] * lax.axis_size("word")), "word", 0
        )
        doc_rhs = doc_sums + doc_plus - dual_doc
        doc_rhs_tile = gathered_copies(doc_rhs, "word", 0)
        inverse_topic = invert(gram_topic)
        doc_factor = product(doc_rhs, inverse_topic)
        doc_tile = product(doc_rhs_tile, inverse_topic)
        gram_doc = exchanged_sum(product_left(doc_tile, doc_tile), "doc")
        inverse_doc = invert(gram_doc)

        def word_term(first_row, row_count, merged=merged, doc_tile=doc_tile):
            return product_left(merged, doc_tile)

        word_sums = summed_on_arrival(
            word_term(jnp.int32(0), topics.shape[0] * lax.axis_size("doc")), "doc", 0
        )
        topic_rhs = word_sums + topic_plus - dual_topic
        topic_rhs_tile = gathered_copies(topic_rhs, "doc", 0)
        topics = product(topic_rhs, inverse_doc)
        topic_tile = product(topic_rhs_tile, inverse_doc)
        rebuilt = product_right(doc_tile, topic_tile)
        shifted = rebuilt - dual_latent - 1.0
        latent = 0.5 * (shifted + jnp.sqrt(shifted * shifted + 4.0 * counts_float))
        doc_plus = jnp.maximum(doc_factor + dual_doc, 0.0)
        topic_plus = jnp.maximum(topics + dual_topic, 0.0)
        dual_latent = dual_latent + latent - rebuilt
        dual_doc = dual_doc + doc_factor - doc_plus
        dual_topic = dual_topic + topics - topic_plus
    return (doc_factor, topics, latent, dual_latent, doc_plus, topic_plus, dual_doc, dual_topic)


def solution(mesh):
    in_specs = (
        P("doc", "word"),
        P(("word", "doc"), None),
        P("doc", "word"),
        P("doc", "word"),
        P(("doc", "word"), None),
        P(("word", "doc"), None),
        P(("doc", "word"), None),
        P(("word", "doc"), None),
    )
    out_specs = (
        P(("doc", "word"), None),
        P(("word", "doc"), None),
        P("doc", "word"),
        P("doc", "word"),
        P(("doc", "word"), None),
        P(("word", "doc"), None),
        P(("doc", "word"), None),
        P(("word", "doc"), None),
    )
    return jax.shard_map(
        per_device, mesh=mesh, in_specs=in_specs, out_specs=out_specs, check_vma=False
    )
```

```python
import jax
import jax.numpy as jnp
from jax import lax
from jax.sharding import PartitionSpec as P

ITERS = 2
NEWTON = 18


def joined_along(pieces, dim):
    pieces = jnp.moveaxis(pieces, 0, dim)
    dims = pieces.shape
    return pieces.reshape(*dims[:dim], dims[dim] * dims[dim + 1], *dims[dim + 2 :])


def copy_for_each(x, axis):
    count = lax.axis_size(axis)
    return lax.all_to_all(jnp.broadcast_to(x[None], (count, *x.shape)), axis, 0, 0, tiled=True)


def gathered_copies(x, axis, dim):
    return joined_along(copy_for_each(x, axis), dim)


def split_up(x, dim, count):
    dims = x.shape
    pieces = x.reshape(*dims[:dim], count, dims[dim] // count, *dims[dim + 1 :])
    return jnp.moveaxis(pieces, dim, 0)


def summed_on_arrival(x, axis, dim):
    count = lax.axis_size(axis)
    pieces = lax.all_to_all(split_up(x, dim, count), axis, 0, 0, tiled=True)
    return jnp.sum(pieces, axis=0)


def rows_for(lines, count):
    spare = -len(lines) % count
    return jnp.pad(lines, [(0, spare)] + [(0, 0)] * (lines.ndim - 1))


def nested_sum(x, axes):
    lines = x.reshape(-1, x.shape[-1])
    own = summed_on_arrival(rows_for(lines, lax.axis_size(axes)), axes, 0)
    whole = gathered_copies(own, axes, 0)
    return whole[: len(lines)].reshape(x.shape)


def exchanged_sum(x, axis):
    count = lax.axis_size(axis)
    bit = 1
    while bit < count:
        x = x + lax.ppermute(x, axis, [(i, i ^ bit) for i in range(count)])
        bit *= 2
    return x


def symmetric_sum(gram, axis):
    half = gram.shape[0] // 2
    upper = exchanged_sum(jnp.concatenate([gram[:half, :], gram[half:, half:]], axis=1), axis)
    top = upper[:, : gram.shape[1]]
    bottom = jnp.concatenate([top[:, half:].T, upper[:, gram.shape[1] :]], axis=1)
    return jnp.concatenate([top, bottom], axis=0)


def product(left, right):
    return jnp.dot(left, right, precision=lax.Precision.HIGHEST, preferred_element_type=jnp.float32)


def product_left(left, right):
    return lax.dot_general(
        left,
        right,
        (((0,), (0,)), ((), ())),
        precision=lax.Precision.HIGHEST,
        preferred_element_type=jnp.float32,
    )


def product_right(left, right):
    return lax.dot_general(
        left,
        right,
        (((1,), (1,)), ((), ())),
        precision=lax.Precision.HIGHEST,
        preferred_element_type=jnp.float32,
    )


def invert(gram):
    identity_mat = jnp.eye(gram.shape[0], dtype=jnp.float32)
    matrix = gram + identity_mat
    row_bound = jnp.max(jnp.sum(jnp.abs(matrix), axis=1))
    approx = identity_mat / row_bound
    for newton_step in range(NEWTON):
        approx = product(approx, 2.0 * identity_mat - product(matrix, approx))
    return approx


def gather_topics(topics):
    return gathered_copies(topics, "doc", 0)


def per_device(counts, topics, latent, dual_latent, doc_plus, topic_plus, dual_doc, dual_topic):
    counts_float = counts.astype(jnp.float32)
    doc_factor = doc_plus
    topic_tile = gather_topics(topics)
    for iteration in range(ITERS):
        merged = latent + dual_latent
        gram_topic = symmetric_sum(product_left(topic_tile, topic_tile), "word")

        def doc_term(first_row, row_count, merged=merged, topic_tile=topic_tile):
            return product(merged, topic_tile)

        doc_sums = summed_on_arrival(
            doc_term(jnp.int32(0), doc_plus.shape[0] * lax.axis_size("word")), "word", 0
        )
        doc_rhs = doc_sums + doc_plus - dual_doc
        doc_rhs_tile = gathered_copies(doc_rhs, "word", 0)
        inverse_topic = invert(gram_topic)
        doc_factor = product(doc_rhs, inverse_topic)
        doc_tile = product(doc_rhs_tile, inverse_topic)
        gram_doc = symmetric_sum(product_left(doc_tile, doc_tile), "doc")
        inverse_doc = invert(gram_doc)

        def word_term(first_row, row_count, merged=merged, doc_tile=doc_tile):
            return product_left(merged, doc_tile)

        word_sums = summed_on_arrival(
            word_term(jnp.int32(0), topics.shape[0] * lax.axis_size("doc")), "doc", 0
        )
        topic_rhs = word_sums + topic_plus - dual_topic
        topic_rhs_tile = gathered_copies(topic_rhs, "doc", 0)
        topics = product(topic_rhs, inverse_doc)
        topic_tile = product(topic_rhs_tile, inverse_doc)
        rebuilt = product_right(doc_tile, topic_tile)
        shifted = rebuilt - dual_latent - 1.0
        latent = 0.5 * (shifted + jnp.sqrt(shifted * shifted + 4.0 * counts_float))
        doc_plus = jnp.maximum(doc_factor + dual_doc, 0.0)
        topic_plus = jnp.maximum(topics + dual_topic, 0.0)
        dual_latent = dual_latent + latent - rebuilt
        dual_doc = dual_doc + doc_factor - doc_plus
        dual_topic = dual_topic + topics - topic_plus
    return (doc_factor, topics, latent, dual_latent, doc_plus, topic_plus, dual_doc, dual_topic)


def solution(mesh):
    in_specs = (
        P("doc", "word"),
        P(("word", "doc"), None),
        P("doc", "word"),
        P("doc", "word"),
        P(("doc", "word"), None),
        P(("word", "doc"), None),
        P(("doc", "word"), None),
        P(("word", "doc"), None),
    )
    out_specs = (
        P(("doc", "word"), None),
        P(("word", "doc"), None),
        P("doc", "word"),
        P("doc", "word"),
        P(("doc", "word"), None),
        P(("word", "doc"), None),
        P(("doc", "word"), None),
        P(("word", "doc"), None),
    )
    return jax.shard_map(
        per_device, mesh=mesh, in_specs=in_specs, out_specs=out_specs, check_vma=False
    )
```

```python
import jax
import jax.numpy as jnp
from jax import lax
from jax.sharding import PartitionSpec as P

ITERS = 2
NEWTON = 18


def joined_along(pieces, dim):
    pieces = jnp.moveaxis(pieces, 0, dim)
    dims = pieces.shape
    return pieces.reshape(*dims[:dim], dims[dim] * dims[dim + 1], *dims[dim + 2 :])


def copy_for_each(x, axis):
    count = lax.axis_size(axis)
    return lax.all_to_all(jnp.broadcast_to(x[None], (count, *x.shape)), axis, 0, 0, tiled=True)


def gathered_copies(x, axis, dim):
    return joined_along(copy_for_each(x, axis), dim)


def split_up(x, dim, count):
    dims = x.shape
    pieces = x.reshape(*dims[:dim], count, dims[dim] // count, *dims[dim + 1 :])
    return jnp.moveaxis(pieces, dim, 0)


def summed_on_arrival(x, axis, dim):
    count = lax.axis_size(axis)
    pieces = lax.all_to_all(split_up(x, dim, count), axis, 0, 0, tiled=True)
    return jnp.sum(pieces, axis=0)


def rows_for(lines, count):
    spare = -len(lines) % count
    return jnp.pad(lines, [(0, spare)] + [(0, 0)] * (lines.ndim - 1))


def nested_sum(x, axes):
    lines = x.reshape(-1, x.shape[-1])
    own = summed_on_arrival(rows_for(lines, lax.axis_size(axes)), axes, 0)
    whole = gathered_copies(own, axes, 0)
    return whole[: len(lines)].reshape(x.shape)


def exchanged_sum(x, axis):
    count = lax.axis_size(axis)
    bit = 1
    while bit < count:
        x = x + lax.ppermute(x, axis, [(i, i ^ bit) for i in range(count)])
        bit *= 2
    return x


def symmetric_sum(gram, axis):
    half = gram.shape[0] // 2
    upper = exchanged_sum(jnp.concatenate([gram[:half, :], gram[half:, half:]], axis=1), axis)
    top = upper[:, : gram.shape[1]]
    bottom = jnp.concatenate([top[:, half:].T, upper[:, gram.shape[1] :]], axis=1)
    return jnp.concatenate([top, bottom], axis=0)


def product(left, right):
    return jnp.dot(left, right, precision=lax.Precision.HIGHEST, preferred_element_type=jnp.float32)


def product_left(left, right):
    return lax.dot_general(
        left,
        right,
        (((0,), (0,)), ((), ())),
        precision=lax.Precision.HIGHEST,
        preferred_element_type=jnp.float32,
    )


def product_right(left, right):
    return lax.dot_general(
        left,
        right,
        (((1,), (1,)), ((), ())),
        precision=lax.Precision.HIGHEST,
        preferred_element_type=jnp.float32,
    )


def invert(gram):
    identity_mat = jnp.eye(gram.shape[0], dtype=jnp.float32)
    matrix = gram + identity_mat
    row_bound = jnp.max(jnp.sum(jnp.abs(matrix), axis=1))
    approx = identity_mat / row_bound
    for newton_step in range(NEWTON):
        approx = product(approx, 2.0 * identity_mat - product(matrix, approx))
    return approx


def gather_topics(topics):
    return gathered_copies(topics, "doc", 0)


def per_device(counts, topics, latent, dual_latent, doc_plus, topic_plus, dual_doc, dual_topic):
    counts_float = counts.astype(jnp.float32)
    doc_factor = doc_plus
    topic_tile = gather_topics(topics)
    for iteration in range(ITERS):
        merged = latent + dual_latent
        gram_topic = exchanged_sum(product_left(topic_tile, topic_tile), "word")

        def doc_term(first_row, row_count, merged=merged, topic_tile=topic_tile):
            return product(merged, topic_tile)

        doc_sums = summed_on_arrival(
            doc_term(jnp.int32(0), doc_plus.shape[0] * lax.axis_size("word")), "word", 0
        )
        doc_rhs = doc_sums + doc_plus - dual_doc
        doc_rhs_tile = gathered_copies(doc_rhs, "word", 0)
        inverse_topic = invert(gram_topic)
        doc_factor = product(doc_rhs, inverse_topic)
        doc_tile = product(doc_rhs_tile, inverse_topic)
        gram_doc = symmetric_sum(product_left(doc_tile, doc_tile), "doc")
        inverse_doc = invert(gram_doc)

        def word_term(first_row, row_count, merged=merged, doc_tile=doc_tile):
            return product_left(merged, doc_tile)

        word_sums = summed_on_arrival(
            word_term(jnp.int32(0), topics.shape[0] * lax.axis_size("doc")), "doc", 0
        )
        topic_rhs = word_sums + topic_plus - dual_topic
        topic_rhs_tile = gathered_copies(topic_rhs, "doc", 0)
        topics = product(topic_rhs, inverse_doc)
        topic_tile = product(topic_rhs_tile, inverse_doc)
        rebuilt = product_right(doc_tile, topic_tile)
        shifted = rebuilt - dual_latent - 1.0
        latent = 0.5 * (shifted + jnp.sqrt(shifted * shifted + 4.0 * counts_float))
        doc_plus = jnp.maximum(doc_factor + dual_doc, 0.0)
        topic_plus = jnp.maximum(topics + dual_topic, 0.0)
        dual_latent = dual_latent + latent - rebuilt
        dual_doc = dual_doc + doc_factor - doc_plus
        dual_topic = dual_topic + topics - topic_plus
    return (doc_factor, topics, latent, dual_latent, doc_plus, topic_plus, dual_doc, dual_topic)


def solution(mesh):
    in_specs = (
        P("doc", "word"),
        P(("word", "doc"), None),
        P("doc", "word"),
        P("doc", "word"),
        P(("doc", "word"), None),
        P(("word", "doc"), None),
        P(("doc", "word"), None),
        P(("word", "doc"), None),
    )
    out_specs = (
        P(("doc", "word"), None),
        P(("word", "doc"), None),
        P("doc", "word"),
        P("doc", "word"),
        P(("doc", "word"), None),
        P(("word", "doc"), None),
        P(("doc", "word"), None),
        P(("word", "doc"), None),
    )
    return jax.shard_map(
        per_device, mesh=mesh, in_specs=in_specs, out_specs=out_specs, check_vma=False
    )
```

```python
import jax
import jax.numpy as jnp
from jax import lax
from jax.sharding import PartitionSpec as P

ITERS = 2
NEWTON = 18


def joined_along(pieces, dim):
    pieces = jnp.moveaxis(pieces, 0, dim)
    dims = pieces.shape
    return pieces.reshape(*dims[:dim], dims[dim] * dims[dim + 1], *dims[dim + 2 :])


def copy_for_each(x, axis):
    count = lax.axis_size(axis)
    return lax.all_to_all(jnp.broadcast_to(x[None], (count, *x.shape)), axis, 0, 0, tiled=True)


def gathered_copies(x, axis, dim):
    return joined_along(copy_for_each(x, axis), dim)


def split_up(x, dim, count):
    dims = x.shape
    pieces = x.reshape(*dims[:dim], count, dims[dim] // count, *dims[dim + 1 :])
    return jnp.moveaxis(pieces, dim, 0)


def summed_on_arrival(x, axis, dim):
    count = lax.axis_size(axis)
    pieces = lax.all_to_all(split_up(x, dim, count), axis, 0, 0, tiled=True)
    return jnp.sum(pieces, axis=0)


def rows_for(lines, count):
    spare = -len(lines) % count
    return jnp.pad(lines, [(0, spare)] + [(0, 0)] * (lines.ndim - 1))


def nested_sum(x, axes):
    lines = x.reshape(-1, x.shape[-1])
    own = summed_on_arrival(rows_for(lines, lax.axis_size(axes)), axes, 0)
    whole = gathered_copies(own, axes, 0)
    return whole[: len(lines)].reshape(x.shape)


def exchanged_sum(x, axis):
    count = lax.axis_size(axis)
    bit = count // 2
    while bit >= 1:
        x = x + lax.ppermute(x, axis, [(i, i ^ bit) for i in range(count)])
        bit //= 2
    return x


def product(left, right):
    return jnp.dot(left, right, precision=lax.Precision.HIGHEST, preferred_element_type=jnp.float32)


def product_left(left, right):
    return lax.dot_general(
        left,
        right,
        (((0,), (0,)), ((), ())),
        precision=lax.Precision.HIGHEST,
        preferred_element_type=jnp.float32,
    )


def product_right(left, right):
    return lax.dot_general(
        left,
        right,
        (((1,), (1,)), ((), ())),
        precision=lax.Precision.HIGHEST,
        preferred_element_type=jnp.float32,
    )


def invert(gram):
    identity_mat = jnp.eye(gram.shape[0], dtype=jnp.float32)
    matrix = gram + identity_mat
    row_bound = jnp.max(jnp.sum(jnp.abs(matrix), axis=1))
    approx = identity_mat / row_bound
    for newton_step in range(NEWTON):
        approx = product(approx, 2.0 * identity_mat - product(matrix, approx))
    return approx


def gather_topics(topics):
    return gathered_copies(topics, "doc", 0)


def per_device(counts, topics, latent, dual_latent, doc_plus, topic_plus, dual_doc, dual_topic):
    counts_float = counts.astype(jnp.float32)
    doc_factor = doc_plus
    topic_tile = gather_topics(topics)
    for iteration in range(ITERS):
        merged = latent + dual_latent
        gram_topic = exchanged_sum(product_left(topic_tile, topic_tile), "word")

        def doc_term(first_row, row_count, merged=merged, topic_tile=topic_tile):
            return product(merged, topic_tile)

        doc_sums = summed_on_arrival(
            doc_term(jnp.int32(0), doc_plus.shape[0] * lax.axis_size("word")), "word", 0
        )
        doc_rhs = doc_sums + doc_plus - dual_doc
        doc_rhs_tile = gathered_copies(doc_rhs, "word", 0)
        inverse_topic = invert(gram_topic)
        doc_factor = product(doc_rhs, inverse_topic)
        doc_tile = product(doc_rhs_tile, inverse_topic)
        gram_doc = exchanged_sum(product_left(doc_tile, doc_tile), "doc")
        inverse_doc = invert(gram_doc)

        def word_term(first_row, row_count, merged=merged, doc_tile=doc_tile):
            return product_left(merged, doc_tile)

        word_sums = summed_on_arrival(
            word_term(jnp.int32(0), topics.shape[0] * lax.axis_size("doc")), "doc", 0
        )
        topic_rhs = word_sums + topic_plus - dual_topic
        topic_rhs_tile = gathered_copies(topic_rhs, "doc", 0)
        topics = product(topic_rhs, inverse_doc)
        topic_tile = product(topic_rhs_tile, inverse_doc)
        rebuilt = product_right(doc_tile, topic_tile)
        shifted = rebuilt - dual_latent - 1.0
        latent = 0.5 * (shifted + jnp.sqrt(shifted * shifted + 4.0 * counts_float))
        doc_plus = jnp.maximum(doc_factor + dual_doc, 0.0)
        topic_plus = jnp.maximum(topics + dual_topic, 0.0)
        dual_latent = dual_latent + latent - rebuilt
        dual_doc = dual_doc + doc_factor - doc_plus
        dual_topic = dual_topic + topics - topic_plus
    return (doc_factor, topics, latent, dual_latent, doc_plus, topic_plus, dual_doc, dual_topic)


def solution(mesh):
    in_specs = (
        P("doc", "word"),
        P(("word", "doc"), None),
        P("doc", "word"),
        P("doc", "word"),
        P(("doc", "word"), None),
        P(("word", "doc"), None),
        P(("doc", "word"), None),
        P(("word", "doc"), None),
    )
    out_specs = (
        P(("doc", "word"), None),
        P(("word", "doc"), None),
        P("doc", "word"),
        P("doc", "word"),
        P(("doc", "word"), None),
        P(("word", "doc"), None),
        P(("doc", "word"), None),
        P(("word", "doc"), None),
    )
    return jax.shard_map(
        per_device, mesh=mesh, in_specs=in_specs, out_specs=out_specs, check_vma=False
    )
```

```python
import jax
import jax.numpy as jnp
from jax import lax
from jax.sharding import PartitionSpec as P

ITERS = 2
NEWTON = 18


def joined_along(pieces, dim):
    pieces = jnp.moveaxis(pieces, 0, dim)
    dims = pieces.shape
    return pieces.reshape(*dims[:dim], dims[dim] * dims[dim + 1], *dims[dim + 2 :])


def copy_for_each(x, axis):
    count = lax.axis_size(axis)
    return lax.all_to_all(jnp.broadcast_to(x[None], (count, *x.shape)), axis, 0, 0, tiled=True)


def gathered_copies(x, axis, dim):
    return joined_along(copy_for_each(x, axis), dim)


def split_up(x, dim, count):
    dims = x.shape
    pieces = x.reshape(*dims[:dim], count, dims[dim] // count, *dims[dim + 1 :])
    return jnp.moveaxis(pieces, dim, 0)


def summed_on_arrival(x, axis, dim):
    count = lax.axis_size(axis)
    pieces = lax.all_to_all(split_up(x, dim, count), axis, 0, 0, tiled=True)
    return jnp.sum(pieces, axis=0)


def rows_for(lines, count):
    spare = -len(lines) % count
    return jnp.pad(lines, [(0, spare)] + [(0, 0)] * (lines.ndim - 1))


def nested_sum(x, axes):
    lines = x.reshape(-1, x.shape[-1])
    own = summed_on_arrival(rows_for(lines, lax.axis_size(axes)), axes, 0)
    whole = gathered_copies(own, axes, 0)
    return whole[: len(lines)].reshape(x.shape)


def exchanged_sum(x, axis):
    count = lax.axis_size(axis)
    bits = [1 << j for j in range(count.bit_length() - 1)]
    for bit in bits if axis == "doc" else bits[::-1]:
        x = x + lax.ppermute(x, axis, [(i, i ^ bit) for i in range(count)])
    return x


def product(left, right):
    return jnp.dot(left, right, precision=lax.Precision.HIGHEST, preferred_element_type=jnp.float32)


def product_left(left, right):
    return lax.dot_general(
        left,
        right,
        (((0,), (0,)), ((), ())),
        precision=lax.Precision.HIGHEST,
        preferred_element_type=jnp.float32,
    )


def product_right(left, right):
    return lax.dot_general(
        left,
        right,
        (((1,), (1,)), ((), ())),
        precision=lax.Precision.HIGHEST,
        preferred_element_type=jnp.float32,
    )


def invert(gram):
    identity_mat = jnp.eye(gram.shape[0], dtype=jnp.float32)
    matrix = gram + identity_mat
    row_bound = jnp.max(jnp.sum(jnp.abs(matrix), axis=1))
    approx = identity_mat / row_bound
    for newton_step in range(NEWTON):
        approx = product(approx, 2.0 * identity_mat - product(matrix, approx))
    return approx


def gather_topics(topics):
    return gathered_copies(topics, "doc", 0)


def per_device(counts, topics, latent, dual_latent, doc_plus, topic_plus, dual_doc, dual_topic):
    counts_float = counts.astype(jnp.float32)
    doc_factor = doc_plus
    topic_tile = gather_topics(topics)
    for iteration in range(ITERS):
        merged = latent + dual_latent
        gram_topic = exchanged_sum(product_left(topic_tile, topic_tile), "word")

        def doc_term(first_row, row_count, merged=merged, topic_tile=topic_tile):
            return product(merged, topic_tile)

        doc_sums = summed_on_arrival(
            doc_term(jnp.int32(0), doc_plus.shape[0] * lax.axis_size("word")), "word", 0
        )
        doc_rhs = doc_sums + doc_plus - dual_doc
        doc_rhs_tile = gathered_copies(doc_rhs, "word", 0)
        inverse_topic = invert(gram_topic)
        doc_factor = product(doc_rhs, inverse_topic)
        doc_tile = product(doc_rhs_tile, inverse_topic)
        gram_doc = exchanged_sum(product_left(doc_tile, doc_tile), "doc")
        inverse_doc = invert(gram_doc)

        def word_term(first_row, row_count, merged=merged, doc_tile=doc_tile):
            return product_left(merged, doc_tile)

        word_sums = summed_on_arrival(
            word_term(jnp.int32(0), topics.shape[0] * lax.axis_size("doc")), "doc", 0
        )
        topic_rhs = word_sums + topic_plus - dual_topic
        topic_rhs_tile = gathered_copies(topic_rhs, "doc", 0)
        topics = product(topic_rhs, inverse_doc)
        topic_tile = product(topic_rhs_tile, inverse_doc)
        rebuilt = product_right(doc_tile, topic_tile)
        shifted = rebuilt - dual_latent - 1.0
        latent = 0.5 * (shifted + jnp.sqrt(shifted * shifted + 4.0 * counts_float))
        doc_plus = jnp.maximum(doc_factor + dual_doc, 0.0)
        topic_plus = jnp.maximum(topics + dual_topic, 0.0)
        dual_latent = dual_latent + latent - rebuilt
        dual_doc = dual_doc + doc_factor - doc_plus
        dual_topic = dual_topic + topics - topic_plus
    return (doc_factor, topics, latent, dual_latent, doc_plus, topic_plus, dual_doc, dual_topic)


def solution(mesh):
    in_specs = (
        P("doc", "word"),
        P(("word", "doc"), None),
        P("doc", "word"),
        P("doc", "word"),
        P(("doc", "word"), None),
        P(("word", "doc"), None),
        P(("doc", "word"), None),
        P(("word", "doc"), None),
    )
    out_specs = (
        P(("doc", "word"), None),
        P(("word", "doc"), None),
        P("doc", "word"),
        P("doc", "word"),
        P(("doc", "word"), None),
        P(("word", "doc"), None),
        P(("doc", "word"), None),
        P(("word", "doc"), None),
    )
    return jax.shard_map(
        per_device, mesh=mesh, in_specs=in_specs, out_specs=out_specs, check_vma=False
    )
```
